512 devices in a mesh: dp: 8 (over y, core), tensor: 64 (over x, z).
Axes of the slice: x: 4, y: 4, z: 16, core: 2. Of those that a mesh axis runs over, the one named last changes fastest.
Arguments:
- hidden: bfloat16 [64, 256, 1536], P('dp', 'tensor'), may hold values from -24 to 24
- norm_gain: float32 [1536], replicated, may hold values from 0.1 to 1.9
- embedding: bfloat16 [49664, 1536], P('tensor'), may hold values from -2 to 2
- targets: int32 [64, 256], P('dp', 'tensor'), may hold values from 0 to 49154
- lengths: int32 [64], replicated, may hold values from 1 to 256, 10240 in all
- loss_mask: int32 [64, 256], P('dp', 'tensor'), may hold values 0 or 1
- deal_slots: int32 [64], replicated, may hold values from 0 to 63, as said below
Outputs:
- log_prob: float32 [64, 256], P('dp', 'tensor')
- entropy: float32 [64, 256], P('dp', 'tensor')
The draws below stay inside these ranges and needn't reach their ends.
Inputs may be any that keep to these rules, and one draw needn't show every extreme that they name: A permutation; sequence k lies in data group deal_slots[k] // 8, and each data group's sequences go in equal numbers to every data group.
All inputs are finite; a program needn't handle non-finite values. No bound on the sum of `loss_mask` on one device may be relied on, other than what follows from the above.
Results may differ from the reference program's by a relative error of at most 0.012.
The reference program's roundings to bfloat16 on the way (of `normed`) count: a program that leaves them out, or rounds other values in their place, can miss the bound.
Values may be sent and summed in bfloat16 or wider, within the bound.
No kernel may reach another device: no remote copies, remote signals or barrier semaphores. Data moves between devices by JAX's collectives and lax.ppermute only.
A program may use at most 64 MiB of HBM per device.

```python
import math
import jax
import jax.numpy as jnp
import numpy as np
from jax import lax

D = 1536
VREAL = 49155
V = 49664
SLOT = 256
SEQ_GROUP = 8
SEQS = 64


def embedding_parts(key):
    base = jax.random.fold_in(key, 11)
    first_key, second_key = jax.random.split(base)
    noise = jnp.clip(jax.random.normal(first_key, (V, D), jnp.float32), -6.0, 6.0)
    scales = jnp.exp(jax.random.uniform(second_key, (V,), jnp.float32, 0.0, math.log(10.0)))
    return (noise, scales)


def draw_embedding(key, part):
    noise, scales = embedding_parts(key)
    return (0.03 * noise * scales[:, None]).astype(jnp.bfloat16)


def draw_hidden(key, part):
    noise = jnp.clip(jax.random.normal(jax.random.fold_in(key, 23), (SEQS, SLOT, D), jnp.float32), -6.0, 6.0)
    return noise.astype(jnp.bfloat16)


def draw_deal_slots(key, part):
    groups = SEQS // SEQ_GROUP
    base = jax.random.fold_in(key, 37)
    group_keys = jax.random.split(jax.random.fold_in(base, 1), groups)
    pattern = jnp.arange(SEQ_GROUP, dtype=jnp.int32) % groups
    destination = jax.vmap(lambda subkey: jax.random.permutation(subkey, pattern))(group_keys).reshape(-1)
    same_group = (destination[:, None] == destination[None, :]).astype(jnp.int32)
    earlier = jnp.sum(jnp.tril(same_group, -1), axis=1)
    slot_keys = jax.random.split(jax.random.fold_in(base, 2), groups)
    shuffles = jax.vmap(lambda subkey: jax.random.permutation(subkey, SEQ_GROUP))(slot_keys).astype(jnp.int32)
    return (destination * SEQ_GROUP + shuffles[destination, earlier]).astype(jnp.int32)


def plant(result, rng, least, high):
    place = [jax.random.randint(jax.random.fold_in(rng, axis), (), 0, length) for axis, length in enumerate(result.shape)]
    widest = result.shape.index(max(result.shape))
    next_to = place[:widest] + [(place[widest] + 1) % result.shape[widest]] + place[widest + 1:]
    return result.at[tuple(place)].set(least).at[tuple(next_to)].set(high)


def rank_bounds(amount, slope):
    loads = [(1 << 20) // math.isqrt(grade ** slope) + 1 for grade in range(1, amount + 1)]
    spread = 1 + sum(loads) // (1 << 30)
    return np.cumsum(np.array([max(1, weight // spread) for weight in loads]))


def ranked(stream_key, dims, count, slope):
    listing = rank_bounds(count, slope)
    ticket = jax.random.randint(jax.random.fold_in(stream_key, 1), dims, 0, int(listing[count - 1]))
    standing = jnp.searchsorted(jnp.asarray(listing, jnp.int32), ticket, side="right")
    return jax.random.permutation(jax.random.fold_in(stream_key, 2), count)[standing].astype(jnp.int32)


def profile(count, total, bound, slope):
    portions = [(1 << 20) // math.isqrt(standing ** slope) + 1 for standing in range(2, count + 1)]
    surplus, given = total - bound - (count - 1), [1] * (count - 1)
    while surplus > 0:
        free = [i for i in range(count - 1) if given[i] < bound]
        whole, remaining = sum([portions[i] for i in free]), surplus
        for i in free:
            extra = min(bound - given[i], max(1, remaining * portions[i] // whole), surplus)
            given[i] = given[i] + extra
            surplus = surplus - extra
    return np.array([bound] + given)


def uneven_parts(rng, count, total, limit, lean):
    if count == 2:
        one = jax.random.randint(rng, (), max(1, total - limit), min(limit, total - 1) + 1)
        return jnp.stack([one, total - one])
    tallies = jnp.asarray(profile(count, total, limit, lean), jnp.int32)
    pairs = (count - 1) // 2
    donor, sink = tallies[1:1 + 2 * pairs:2], tallies[2:2 + 2 * pairs:2]
    slack = jnp.minimum(donor - 1, limit - sink)
    moved = jax.random.randint(jax.random.fold_in(rng, 1), (pairs,), 0, 1 << 20) % (slack + 1)
    tallies = tallies.at[1:1 + 2 * pairs:2].set(donor - moved).at[2:2 + 2 * pairs:2].set(sink + moved)
    return tallies[jax.random.permutation(jax.random.fold_in(rng, 2), count)]


def setup_inputs(seed: int = 0) -> dict:
    splits = jax.random.split(jax.random.key(seed), 8)
    hidden = draw_hidden(jax.random.fold_in(splits[7], 71), 0)
    norm_gain = jnp.clip(1.0 + 0.18 * jax.random.normal(splits[1], (D,), jnp.float32), 0.1, 1.9)
    embedding = draw_embedding(jax.random.fold_in(splits[7], 71), 0)
    targets = plant(ranked(splits[3], (SEQS, SLOT), VREAL, 2), jax.random.fold_in(splits[3], 3), 0, VREAL - 1).astype(jnp.int32)
    lengths = uneven_parts(splits[4], SEQS, SEQS * SLOT * 5 // 8, SLOT, 2).astype(jnp.int32)
    loss_mask = plant((jax.random.randint(splits[5], (SEQS, SLOT), 0, 4) < 3).astype(jnp.int32), jax.random.fold_in(splits[5], 1), 0, 1)
    deal_slots = draw_deal_slots(jax.random.fold_in(splits[7], 71), 0)
    return dict(hidden=hidden, norm_gain=norm_gain, embedding=embedding, targets=targets, lengths=lengths, loss_mask=loss_mask, deal_slots=deal_slots)


def reference(hidden, norm_gain, embedding, targets, lengths, loss_mask, deal_slots):
    source = hidden[deal_slots]

    def per_sequence(inputs):
        rows, wanted, length, marks = inputs
        values = rows.astype(jnp.float32)
        inverse = lax.rsqrt(lax.optimization_barrier(jnp.mean(values * values, axis=1, keepdims=True)) + 1e-05)
        normed = (values * inverse * norm_gain).astype(jnp.bfloat16)
        logits = jnp.dot(normed, embedding.T, preferred_element_type=jnp.float32)
        columns = jnp.arange(V, dtype=jnp.int32)
        usable = columns[None, :] < VREAL
        maximum = lax.optimization_barrier(jnp.max(jnp.where(usable, logits, -jnp.inf), axis=1))
        weights = jnp.where(usable, jnp.exp(logits - maximum[:, None]), 0.0)
        totals = lax.optimization_barrier(jnp.sum(weights, axis=1))
        weighted = lax.optimization_barrier(jnp.sum(weights * jnp.where(usable, logits, 0.0), axis=1))
        log_total = maximum + jnp.log(totals)
        chosen = jnp.take_along_axis(logits, wanted[:, None].astype(jnp.int32), axis=1)[:, 0]
        positions = jnp.arange(SLOT, dtype=jnp.int32)
        scored = (positions < length) & (marks == 1)
        log_prob = jnp.where(scored, chosen - log_total, 0.0)
        entropy = jnp.where(scored, log_total - weighted / totals, 0.0)
        return (log_prob, entropy)
    log_prob, entropy = lax.map(per_sequence, (source, targets, lengths, loss_mask))
    return (log_prob, entropy)
```

```python
import numpy as np
import jax
import jax.numpy as jnp
from jax import lax
from jax.sharding import Mesh
from jax.sharding import PartitionSpec as P

VREAL = 49155


def normalize(hidden, norm_gain):
    values = hidden.astype(jnp.float32)
    inverse = lax.rsqrt(jnp.mean(values * values, axis=2, keepdims=True) + 1e-05)
    return (values * inverse * norm_gain).astype(jnp.bfloat16)


def split_tensor(mesh):
    row = mesh.devices[0]
    slow = len({tuple(d.coords)[0] for d in row})
    if row.size % slow or slow in (1, row.size):
        return None
    return slow, row.size // slow


def local_fn(tensor_axes, tensor_size):
    def tensor_rank():
        if len(tensor_axes) == 1:
            return lax.axis_index(tensor_axes[0])
        return lax.axis_index(tensor_axes[0]) * tensor_size[1] + lax.axis_index(tensor_axes[1])

    def gather_rows(normed):
        rows = normed
        for name in tensor_axes:
            rows = lax.all_gather(rows, name, axis=1, tiled=True)
        return rows

    def to_gather_order(by_rank):
        s, w = by_rank.shape[1], by_rank.shape[2]
        if len(tensor_axes) == 1:
            return jnp.transpose(by_rank, (1, 0, 2)).reshape(-1)
        grid = by_rank.reshape(tensor_size[0], tensor_size[1], s, w)
        return jnp.transpose(grid, (2, 1, 0, 3)).reshape(-1)

    def from_gather_order(stats, s, w):
        k = stats.shape[0]
        if len(tensor_axes) == 1:
            return jnp.transpose(stats.reshape(k, s, tensor_size[0], w), (2, 0, 1, 3))
        grid = stats.reshape(k, s, tensor_size[1], tensor_size[0], w)
        grid = jnp.transpose(grid, (3, 2, 0, 1, 4))
        return grid.reshape(tensor_size[0] * tensor_size[1], k, s, w)

    def local(hidden, norm_gain, embedding, targets, lengths, loss_mask, deal_slots):
        group_rank = lax.axis_index("dp")
        sequences, row_width = hidden.shape[0], hidden.shape[1]
        ranks = int(np.prod(tensor_size))
        t_rank = tensor_rank()
        owned_seqs = group_rank * sequences + jnp.arange(sequences, dtype=jnp.int32)
        destination = deal_slots[owned_seqs] // sequences
        send_order = jnp.argsort(destination, stable=True)
        every_group = deal_slots // sequences
        arrived = jnp.argsort((every_group != group_rank).astype(jnp.int32), stable=True)[:sequences]
        arrived_slot = deal_slots[arrived] % sequences
        positions = t_rank * row_width + jnp.arange(row_width, dtype=jnp.int32)
        scored = (positions[None, :] < lengths[owned_seqs][:, None]) & (loss_mask == 1)
        marked = jnp.where(scored, targets, -1)
        undo_order = jnp.argsort(send_order)

        normed = normalize(hidden, norm_gain)
        row_block = gather_rows(normed)

        came = lax.all_to_all(marked[send_order], "dp", split_axis=0, concat_axis=0, tiled=True)
        worker_marks = came[jnp.argsort(arrived_slot)]
        spread = jnp.broadcast_to(worker_marks[None], (ranks,) + worker_marks.shape)
        block_marks = lax.all_to_all(spread, tensor_axes, split_axis=0, concat_axis=0, tiled=True)
        block_marks = to_gather_order(block_marks)

        vocab_rows = embedding.shape[0]
        columns = t_rank * vocab_rows + jnp.arange(vocab_rows, dtype=jnp.int32)
        usable = columns < VREAL
        flat_rows = row_block.reshape(-1, row_block.shape[2])
        logits = jnp.einsum("nd,vd->nv", flat_rows, embedding, preferred_element_type=jnp.float32)
        maximum = jnp.max(jnp.where(usable, logits, -jnp.inf), axis=1)
        weights = jnp.where(usable, jnp.exp(logits - maximum[:, None]), 0.0)
        totals = jnp.sum(weights, axis=1)
        weighted = jnp.sum(weights * jnp.where(usable, logits, 0.0), axis=1)
        chosen = jnp.sum(jnp.where(columns[None, :] == block_marks[:, None], logits, 0.0), axis=1)

        stats = from_gather_order(jnp.stack([maximum, totals, weighted, chosen]), sequences, row_width)
        parts = lax.all_to_all(stats, tensor_axes, split_axis=0, concat_axis=0, tiled=True)
        part_max, part_tot, part_wt, part_ch = parts[:, 0], parts[:, 1], parts[:, 2], parts[:, 3]
        overall = jnp.max(part_max, axis=0)
        factor = jnp.exp(part_max - overall[None])
        totals = jnp.sum(part_tot * factor, axis=0)
        weighted = jnp.sum(part_wt * factor, axis=0)
        chosen = jnp.sum(part_ch, axis=0)
        log_total = overall + jnp.log(totals)
        usable_rows = worker_marks >= 0
        log_prob = jnp.where(usable_rows, chosen - log_total, 0.0)
        entropy = jnp.where(usable_rows, log_total - weighted / totals, 0.0)

        both = jnp.stack([log_prob, entropy], axis=1)[arrived_slot]
        returned = lax.all_to_all(both, "dp", split_axis=0, concat_axis=0, tiled=True)[undo_order]
        return returned[:, 0], returned[:, 1]

    return local


def solution(mesh):
    split = split_tensor(mesh)
    if split is None:
        run_mesh, tensor_axes, tensor_size = mesh, ("tensor",), (mesh.shape["tensor"],)
    else:
        dp = mesh.shape["dp"]
        run_mesh = Mesh(mesh.devices.reshape(dp, split[0], split[1]), ("dp", "tx", "tz"))
        tensor_axes, tensor_size = ("tx", "tz"), split
    tensor = tensor_axes if len(tensor_axes) > 1 else tensor_axes[0]
    placed = (
        P("dp", tensor, None),
        P(),
        P(tensor, None),
        P("dp", tensor),
        P(),
        P("dp", tensor),
        P(),
    )
    return jax.shard_map(
        local_fn(tensor_axes, tensor_size),
        mesh=run_mesh,
        in_specs=placed,
        out_specs=(P("dp", tensor), P("dp", tensor)),
        check_vma=False,
    )
```

```python
import numpy as np
import jax
import jax.numpy as jnp
from jax import lax
from jax.experimental import pallas as pl
from jax.experimental.pallas import tpu as pltpu
from jax.sharding import Mesh
from jax.sharding import PartitionSpec as P

VREAL = 49155
INTERPRET = False
ROW_BLOCK = 256


def stats_kernel(offset_ref, rows_ref, emb_ref, marks_ref, out_ref):
    logits = lax.dot_general(
        rows_ref[...], emb_ref[...], (((1,), (1,)), ((), ())), preferred_element_type=jnp.float32
    )
    columns = offset_ref[0] + lax.broadcasted_iota(jnp.int32, logits.shape, 1)
    usable = columns < VREAL
    maximum = jnp.max(jnp.where(usable, logits, -jnp.inf), axis=1, keepdims=True)
    weights = jnp.where(usable, jnp.exp(logits - maximum), 0.0)
    totals = jnp.sum(weights, axis=1, keepdims=True)
    weighted = jnp.sum(weights * jnp.where(usable, logits, 0.0), axis=1, keepdims=True)
    chosen = jnp.sum(jnp.where(columns == marks_ref[...], logits, 0.0), axis=1, keepdims=True)
    out_ref[...] = jnp.concatenate([maximum, totals, weighted, chosen], axis=1)


def row_stats(rows, embedding, marks, offset):
    n, d = rows.shape
    v = embedding.shape[0]
    block = ROW_BLOCK if n % ROW_BLOCK == 0 else n
    return pl.pallas_call(
        stats_kernel,
        grid=(n // block,),
        in_specs=[
            pl.BlockSpec(memory_space=pltpu.SMEM),
            pl.BlockSpec((block, d), lambda i: (i, 0)),
            pl.BlockSpec((v, d), lambda i: (0, 0)),
            pl.BlockSpec((block, 1), lambda i: (i, 0)),
        ],
        out_specs=pl.BlockSpec((block, 4), lambda i: (i, 0)),
        out_shape=jax.ShapeDtypeStruct((n, 4), jnp.float32),
        cost_estimate=pl.CostEstimate(
            flops=2 * n * v * d, transcendentals=n * v, bytes_accessed=2 * (n + v) * d + 20 * n
        ),
        interpret=INTERPRET,
    )(offset.reshape(1), rows, embedding, marks.reshape(n, 1))


def normalize(hidden, norm_gain):
    values = hidden.astype(jnp.float32)
    inverse = lax.rsqrt(jnp.mean(values * values, axis=2, keepdims=True) + 1e-05)
    return (values * inverse * norm_gain).astype(jnp.bfloat16)


def split_tensor(mesh):
    row = mesh.devices[0]
    slow = len({tuple(d.coords)[0] for d in row})
    if row.size % slow or slow in (1, row.size):
        return None
    return slow, row.size // slow


def local_fn(tensor_axes, tensor_size):
    def tensor_rank():
        if len(tensor_axes) == 1:
            return lax.axis_index(tensor_axes[0])
        return lax.axis_index(tensor_axes[0]) * tensor_size[1] + lax.axis_index(tensor_axes[1])

    def gather_rows(normed):
        rows = normed
        for name in tensor_axes:
            rows = lax.all_gather(rows, name, axis=1, tiled=True)
        return rows

    def to_gather_order(by_rank):
        s, w = by_rank.shape[1], by_rank.shape[2]
        if len(tensor_axes) == 1:
            return jnp.transpose(by_rank, (1, 0, 2)).reshape(-1)
        grid = by_rank.reshape(tensor_size[0], tensor_size[1], s, w)
        return jnp.transpose(grid, (2, 1, 0, 3)).reshape(-1)

    def from_gather_order(stats, s, w):
        k = stats.shape[0]
        if len(tensor_axes) == 1:
            return jnp.transpose(stats.reshape(k, s, tensor_size[0], w), (2, 0, 1, 3))
        grid = stats.reshape(k, s, tensor_size[1], tensor_size[0], w)
        grid = jnp.transpose(grid, (3, 2, 0, 1, 4))
        return grid.reshape(tensor_size[0] * tensor_size[1], k, s, w)

    def local(hidden, norm_gain, embedding, targets, lengths, loss_mask, deal_slots):
        group_rank = lax.axis_index("dp")
        sequences, row_width = hidden.shape[0], hidden.shape[1]
        ranks = int(np.prod(tensor_size))
        t_rank = tensor_rank()
        owned_seqs = group_rank * sequences + jnp.arange(sequences, dtype=jnp.int32)
        destination = deal_slots[owned_seqs] // sequences
        send_order = jnp.argsort(destination, stable=True)
        every_group = deal_slots // sequences
        arrived = jnp.argsort((every_group != group_rank).astype(jnp.int32), stable=True)[:sequences]
        arrived_slot = deal_slots[arrived] % sequences
        positions = t_rank * row_width + jnp.arange(row_width, dtype=jnp.int32)
        scored = (positions[None, :] < lengths[owned_seqs][:, None]) & (loss_mask == 1)
        marked = jnp.where(scored, targets, -1)
        undo_order = jnp.argsort(send_order)

        normed = normalize(hidden, norm_gain)
        row_block = gather_rows(normed)

        came = lax.all_to_all(marked[send_order], "dp", split_axis=0, concat_axis=0, tiled=True)
        worker_marks = came[jnp.argsort(arrived_slot)]
        spread = jnp.broadcast_to(worker_marks[None], (ranks,) + worker_marks.shape)
        block_marks = lax.all_to_all(spread, tensor_axes, split_axis=0, concat_axis=0, tiled=True)
        block_marks = to_gather_order(block_marks)

        offset = (t_rank * embedding.shape[0]).astype(jnp.int32)
        flat_rows = row_block.reshape(-1, row_block.shape[2])
        local_stats = row_stats(flat_rows, embedding, block_marks, offset)

        stats = from_gather_order(jnp.transpose(local_stats), sequences, row_width)
        parts = lax.all_to_all(stats, tensor_axes, split_axis=0, concat_axis=0, tiled=True)
        part_max, part_tot, part_wt, part_ch = parts[:, 0], parts[:, 1], parts[:, 2], parts[:, 3]
        overall = jnp.max(part_max, axis=0)
        factor = jnp.exp(part_max - overall[None])
        totals = jnp.sum(part_tot * factor, axis=0)
        weighted = jnp.sum(part_wt * factor, axis=0)
        chosen = jnp.sum(part_ch, axis=0)
        log_total = overall + jnp.log(totals)
        usable_rows = worker_marks >= 0
        log_prob = jnp.where(usable_rows, chosen - log_total, 0.0)
        entropy = jnp.where(usable_rows, log_total - weighted / totals, 0.0)

        both = jnp.stack([log_prob, entropy], axis=1)[arrived_slot]
        returned = lax.all_to_all(both, "dp", split_axis=0, concat_axis=0, tiled=True)[undo_order]
        return returned[:, 0], returned[:, 1]

    return local


def solution(mesh):
    split = split_tensor(mesh)
    if split is None:
        run_mesh, tensor_axes, tensor_size = mesh, ("tensor",), (mesh.shape["tensor"],)
    else:
        dp = mesh.shape["dp"]
        run_mesh = Mesh(mesh.devices.reshape(dp, split[0], split[1]), ("dp", "tx", "tz"))
        tensor_axes, tensor_size = ("tx", "tz"), split
    tensor = tensor_axes if len(tensor_axes) > 1 else tensor_axes[0]
    placed = (
        P("dp", tensor, None),
        P(),
        P(tensor, None),
        P("dp", tensor),
        P(),
        P("dp", tensor),
        P(),
    )
    return jax.shard_map(
        local_fn(tensor_axes, tensor_size),
        mesh=run_mesh,
        in_specs=placed,
        out_specs=(P("dp", tensor), P("dp", tensor)),
        check_vma=False,
    )
```

```python
import numpy as np
import jax
import jax.numpy as jnp
from jax import lax
from jax.experimental import pallas as pl
from jax.experimental.pallas import tpu as pltpu
from jax.sharding import Mesh
from jax.sharding import PartitionSpec as P

VREAL = 49155
INTERPRET = False
ROW_BLOCK = 256


def stats_kernel(offset_ref, rows_ref, emb_ref, marks_ref, out_ref):
    logits = jnp.dot(rows_ref[...], emb_ref[...], preferred_element_type=jnp.float32)
    columns = offset_ref[0] + lax.broadcasted_iota(jnp.int32, logits.shape, 1)
    usable = columns < VREAL
    maximum = jnp.max(jnp.where(usable, logits, -jnp.inf), axis=1, keepdims=True)
    weights = jnp.where(usable, jnp.exp(logits - maximum), 0.0)
    totals = jnp.sum(weights, axis=1, keepdims=True)
    weighted = jnp.sum(weights * jnp.where(usable, logits, 0.0), axis=1, keepdims=True)
    chosen = jnp.sum(jnp.where(columns == marks_ref[...], logits, 0.0), axis=1, keepdims=True)
    out_ref[...] = jnp.concatenate([maximum, totals, weighted, chosen], axis=1)


def row_stats(rows, emb_t, marks, offset):
    n, d = rows.shape
    v = emb_t.shape[1]
    block = ROW_BLOCK if n % ROW_BLOCK == 0 else n
    return pl.pallas_call(
        stats_kernel,
        grid=(n // block,),
        in_specs=[
            pl.BlockSpec(memory_space=pltpu.SMEM),
            pl.BlockSpec((block, d), lambda i: (i, 0)),
            pl.BlockSpec((d, v), lambda i: (0, 0)),
            pl.BlockSpec((block, 1), lambda i: (i, 0)),
        ],
        out_specs=pl.BlockSpec((block, 4), lambda i: (i, 0)),
        out_shape=jax.ShapeDtypeStruct((n, 4), jnp.float32),
        cost_estimate=pl.CostEstimate(
            flops=2 * n * v * d, transcendentals=n * v, bytes_accessed=2 * (n + v) * d + 20 * n
        ),
        interpret=INTERPRET,
    )(offset.reshape(1), rows, emb_t, marks.reshape(n, 1))


def normalize(hidden, norm_gain):
    values = hidden.astype(jnp.float32)
    inverse = lax.rsqrt(jnp.mean(values * values, axis=2, keepdims=True) + 1e-05)
    return (values * inverse * norm_gain).astype(jnp.bfloat16)


def split_tensor(mesh):
    row = mesh.devices[0]
    slow = len({tuple(d.coords)[0] for d in row})
    if row.size % slow or slow in (1, row.size):
        return None
    return slow, row.size // slow


def local_fn(tensor_axes, tensor_size):
    def tensor_rank():
        if len(tensor_axes) == 1:
            return lax.axis_index(tensor_axes[0])
        return lax.axis_index(tensor_axes[0]) * tensor_size[1] + lax.axis_index(tensor_axes[1])

    def gather_rows(normed):
        rows = normed
        for name in tensor_axes:
            rows = lax.all_gather(rows, name, axis=1, tiled=True)
        return rows

    def to_gather_order(by_rank):
        s, w = by_rank.shape[1], by_rank.shape[2]
        if len(tensor_axes) == 1:
            return jnp.transpose(by_rank, (0, 2, 1)).reshape(-1)
        grid = by_rank.reshape(tensor_size[0], tensor_size[1], s, w)
        return jnp.transpose(grid, (1, 0, 3, 2)).reshape(-1)

    def from_gather_order(stats, s, w):
        k = stats.shape[0]
        if len(tensor_axes) == 1:
            return jnp.transpose(stats.reshape(k, tensor_size[0], w, s), (1, 0, 3, 2))
        grid = stats.reshape(k, tensor_size[1], tensor_size[0], w, s)
        grid = jnp.transpose(grid, (2, 1, 0, 4, 3))
        return grid.reshape(tensor_size[0] * tensor_size[1], k, s, w)

    def local(hidden, norm_gain, embedding, targets, lengths, loss_mask, deal_slots):
        group_rank = lax.axis_index("dp")
        sequences, row_width = hidden.shape[0], hidden.shape[1]
        ranks = int(np.prod(tensor_size))
        t_rank = tensor_rank()
        owned_seqs = group_rank * sequences + jnp.arange(sequences, dtype=jnp.int32)
        destination = deal_slots[owned_seqs] // sequences
        send_order = jnp.argsort(destination, stable=True)
        every_group = deal_slots // sequences
        arrived = jnp.argsort((every_group != group_rank).astype(jnp.int32), stable=True)[:sequences]
        arrived_slot = deal_slots[arrived] % sequences
        positions = t_rank * row_width + jnp.arange(row_width, dtype=jnp.int32)
        scored = (positions[None, :] < lengths[owned_seqs][:, None]) & (loss_mask == 1)
        marked = jnp.where(scored, targets, -1)
        undo_order = jnp.argsort(send_order)

        normed = normalize(hidden, norm_gain)
        row_block = gather_rows(normed)

        came = lax.all_to_all(marked[send_order], "dp", split_axis=0, concat_axis=0, tiled=True)
        worker_marks = came[jnp.argsort(arrived_slot)]
        spread = jnp.broadcast_to(worker_marks[None], (ranks,) + worker_marks.shape)
        block_marks = lax.all_to_all(spread, tensor_axes, split_axis=0, concat_axis=0, tiled=True)
        block_marks = to_gather_order(block_marks)

        offset = (t_rank * embedding.shape[0]).astype(jnp.int32)
        flat_rows = jnp.transpose(row_block, (1, 0, 2)).reshape(-1, row_block.shape[2])
        local_stats = row_stats(flat_rows, jnp.transpose(embedding), block_marks, offset)

        stats = from_gather_order(jnp.transpose(local_stats), sequences, row_width)
        parts = lax.all_to_all(stats, tensor_axes, split_axis=0, concat_axis=0, tiled=True)
        part_max, part_tot, part_wt, part_ch = parts[:, 0], parts[:, 1], parts[:, 2], parts[:, 3]
        overall = jnp.max(part_max, axis=0)
        factor = jnp.exp(part_max - overall[None])
        totals = jnp.sum(part_tot * factor, axis=0)
        weighted = jnp.sum(part_wt * factor, axis=0)
        chosen = jnp.sum(part_ch, axis=0)
        log_total = overall + jnp.log(totals)
        usable_rows = worker_marks >= 0
        log_prob = jnp.where(usable_rows, chosen - log_total, 0.0)
        entropy = jnp.where(usable_rows, log_total - weighted / totals, 0.0)

        both = jnp.stack([log_prob, entropy], axis=1)[arrived_slot]
        returned = lax.all_to_all(both, "dp", split_axis=0, concat_axis=0, tiled=True)[undo_order]
        return returned[:, 0], returned[:, 1]

    return local


def solution(mesh):
    split = split_tensor(mesh)
    if split is None:
        run_mesh, tensor_axes, tensor_size = mesh, ("tensor",), (mesh.shape["tensor"],)
    else:
        dp = mesh.shape["dp"]
        run_mesh = Mesh(mesh.devices.reshape(dp, split[0], split[1]), ("dp", "tx", "tz"))
        tensor_axes, tensor_size = ("tx", "tz"), split
    tensor = tensor_axes if len(tensor_axes) > 1 else tensor_axes[0]
    placed = (
        P("dp", tensor, None),
        P(),
        P(tensor, None),
        P("dp", tensor),
        P(),
        P("dp", tensor),
        P(),
    )
    return jax.shard_map(
        local_fn(tensor_axes, tensor_size),
        mesh=run_mesh,
        in_specs=placed,
        out_specs=(P("dp", tensor), P("dp", tensor)),
        check_vma=False,
    )
```

```python
import numpy as np
import jax
import jax.numpy as jnp
from jax import lax
from jax.experimental import pallas as pl
from jax.experimental.pallas import tpu as pltpu
from jax.sharding import Mesh
from jax.sharding import PartitionSpec as P

VREAL = 49155
INTERPRET = False
ROW_BLOCK = 256


def stats_kernel(offset_ref, rows_ref, emb_ref, marks_ref, out_ref):
    logits = jnp.dot(rows_ref[...], emb_ref[...], preferred_element_type=jnp.float32)
    columns = offset_ref[0] + lax.broadcasted_iota(jnp.int32, logits.shape, 1)
    write_stats(logits, columns, marks_ref, out_ref)


def ids_kernel(ids_ref, rows_ref, emb_ref, marks_ref, out_ref):
    logits = lax.dot_general(
        rows_ref[...], emb_ref[...], (((1,), (1,)), ((), ())), preferred_element_type=jnp.float32
    )
    write_stats(logits, ids_ref[...], marks_ref, out_ref)


def write_stats(logits, columns, marks_ref, out_ref):
    usable = columns < VREAL
    maximum = jnp.max(jnp.where(usable, logits, -jnp.inf), axis=1, keepdims=True)
    weights = jnp.where(usable, jnp.exp(logits - maximum), 0.0)
    totals = jnp.sum(weights, axis=1, keepdims=True)
    weighted = jnp.sum(weights * jnp.where(usable, logits, 0.0), axis=1, keepdims=True)
    chosen = jnp.sum(jnp.where(columns == marks_ref[...], logits, 0.0), axis=1, keepdims=True)
    out_ref[...] = jnp.concatenate([maximum, totals, weighted, chosen], axis=1)


def row_stats(rows, emb_t, marks, offset):
    n, d = rows.shape
    v = emb_t.shape[1]
    block = ROW_BLOCK if n % ROW_BLOCK == 0 else n
    return pl.pallas_call(
        stats_kernel,
        grid=(n // block,),
        in_specs=[
            pl.BlockSpec(memory_space=pltpu.SMEM),
            pl.BlockSpec((block, d), lambda i: (i, 0)),
            pl.BlockSpec((d, v), lambda i: (0, 0)),
            pl.BlockSpec((block, 1), lambda i: (i, 0)),
        ],
        out_specs=pl.BlockSpec((block, 4), lambda i: (i, 0)),
        out_shape=jax.ShapeDtypeStruct((n, 4), jnp.float32),
        cost_estimate=pl.CostEstimate(
            flops=2 * n * v * d, transcendentals=n * v, bytes_accessed=2 * (n + v) * d + 20 * n
        ),
        interpret=INTERPRET,
    )(offset.reshape(1), rows, emb_t, marks.reshape(n, 1))


def id_stats(rows, table, ids, marks):
    n, d = rows.shape
    v = table.shape[0]
    block = ROW_BLOCK if n % ROW_BLOCK == 0 else n
    return pl.pallas_call(
        ids_kernel,
        grid=(n // block,),
        in_specs=[
            pl.BlockSpec((1, v), lambda i: (0, 0)),
            pl.BlockSpec((block, d), lambda i: (i, 0)),
            pl.BlockSpec((v, d), lambda i: (0, 0)),
            pl.BlockSpec((block, 1), lambda i: (i, 0)),
        ],
        out_specs=pl.BlockSpec((block, 4), lambda i: (i, 0)),
        out_shape=jax.ShapeDtypeStruct((n, 4), jnp.float32),
        cost_estimate=pl.CostEstimate(
            flops=2 * n * v * d, transcendentals=n * v, bytes_accessed=2 * (n + v) * d + 20 * n
        ),
        interpret=INTERPRET,
    )(ids.reshape(1, v), rows, table, marks.reshape(n, 1))


def merge_stats(parts, axis):
    part_max, part_tot, part_wt, part_ch = [lax.index_in_dim(parts, i, axis=-1, keepdims=False) for i in range(4)]
    overall = jnp.max(part_max, axis=axis, keepdims=True)
    factor = jnp.exp(part_max - overall)
    return jnp.stack([
        jnp.squeeze(overall, axis),
        jnp.sum(part_tot * factor, axis=axis),
        jnp.sum(part_wt * factor, axis=axis),
        jnp.sum(part_ch, axis=axis),
    ], axis=-1)


def plane_fn(sizes):
    n_ty, n_tc, n_tx, n_tz = sizes
    dp_axes = ("ty", "tc")

    def local(hidden, norm_gain, embedding, targets, lengths, loss_mask, deal_slots):
        group_rank = lax.axis_index("ty") * n_tc + lax.axis_index("tc")
        core = lax.axis_index("tc")
        xr, zr = lax.axis_index("tx"), lax.axis_index("tz")
        sequences, row_width = hidden.shape[0], hidden.shape[1]
        vocab_rows, width = embedding.shape

        half = vocab_rows // n_tc
        mine = lax.dynamic_slice_in_dim(embedding, core * half, half, 0)
        fetched, sources = [], []
        for step in range(1, n_tx // 2 + 1):
            if 2 * step == n_tx:
                quarter = half // 2
                fetched.append(lax.ppermute(mine[:quarter], "tx", [(i, (i + step) % n_tx) for i in range(n_tx)]))
                fetched.append(lax.ppermute(mine[quarter:], "tx", [(i, (i - step) % n_tx) for i in range(n_tx)]))
                sources.append((-step, 0, quarter))
                sources.append((step, quarter, half))
            else:
                fetched.append(lax.ppermute(mine, "tx", [(i, (i + step) % n_tx) for i in range(n_tx)]))
                fetched.append(lax.ppermute(mine, "tx", [(i, (i - step) % n_tx) for i in range(n_tx)]))
                sources.append((-step, 0, half))
                sources.append((step, 0, half))
        got = jnp.concatenate(fetched, 0)
        other = lax.ppermute(got, "tc", [(i, (i + 1) % n_tc) for i in range(n_tc)]) if n_tc == 2 else None
        got_ids = []
        for shift, lo, hi in sources:
            rank = ((xr + shift) % n_tx) * n_tz + zr
            got_ids.append(rank * vocab_rows + jnp.arange(lo, hi, dtype=jnp.int32))
        got_ids = jnp.concatenate(got_ids)
        mine_ids = got_ids + core * half
        other_ids = got_ids + (1 - core) * half

        owned_seqs = group_rank * sequences + jnp.arange(sequences, dtype=jnp.int32)
        destination = deal_slots[owned_seqs] // sequences
        send_order = jnp.argsort(destination, stable=True)
        every_group = deal_slots // sequences
        arrived = jnp.argsort((every_group != group_rank).astype(jnp.int32), stable=True)[:sequences]
        arrived_slot = deal_slots[arrived] % sequences
        positions = (xr * n_tz + zr) * row_width + jnp.arange(row_width, dtype=jnp.int32)
        scored = (positions[None, :] < lengths[owned_seqs][:, None]) & (loss_mask == 1)
        marked = jnp.where(scored, targets, -1)
        undo_order = jnp.argsort(send_order)

        normed = normalize(hidden, norm_gain)
        row_block = lax.all_gather(normed, "tz", axis=1, tiled=True)

        came = lax.all_to_all(marked[send_order], dp_axes, split_axis=0, concat_axis=0, tiled=True)
        worker_marks = came[jnp.argsort(arrived_slot)]
        spread = jnp.broadcast_to(worker_marks[None], (n_tz,) + worker_marks.shape)
        block_marks = lax.all_to_all(spread, "tz", split_axis=0, concat_axis=0, tiled=True)
        block_marks = jnp.transpose(block_marks, (0, 2, 1)).reshape(-1)

        flat_rows = jnp.transpose(row_block, (1, 0, 2)).reshape(-1, width)
        own_ids = (xr * n_tz + zr) * vocab_rows + jnp.arange(vocab_rows, dtype=jnp.int32)
        parts = [
            id_stats(flat_rows, embedding, own_ids, block_marks),
            id_stats(flat_rows, got, mine_ids, block_marks),
        ]
        if other is not None:
            parts.append(id_stats(flat_rows, other, other_ids, block_marks))
        local_stats = merge_stats(jnp.stack(parts), 0)

        stats = jnp.transpose(local_stats.reshape(n_tz, row_width, sequences, 4), (0, 3, 2, 1))
        parts = lax.all_to_all(stats, "tz", split_axis=0, concat_axis=0, tiled=True)
        merged = merge_stats(jnp.transpose(parts, (0, 2, 3, 1)), 0)
        overall, totals, weighted, chosen = [merged[..., i] for i in range(4)]
        log_total = overall + jnp.log(totals)
        usable_rows = worker_marks >= 0
        log_prob = jnp.where(usable_rows, chosen - log_total, 0.0)
        entropy = jnp.where(usable_rows, log_total - weighted / totals, 0.0)

        both = jnp.stack([log_prob, entropy], axis=1)[arrived_slot]
        returned = lax.all_to_all(both, dp_axes, split_axis=0, concat_axis=0, tiled=True)[undo_order]
        return returned[:, 0], returned[:, 1]

    return local


def normalize(hidden, norm_gain):
    values = hidden.astype(jnp.float32)
    inverse = lax.rsqrt(jnp.mean(values * values, axis=2, keepdims=True) + 1e-05)
    return (values * inverse * norm_gain).astype(jnp.bfloat16)


def split_tensor(mesh):
    row = mesh.devices[0]
    slow = len({tuple(d.coords)[0] for d in row})
    if row.size % slow or slow in (1, row.size):
        return None
    return slow, row.size // slow


def local_fn(tensor_axes, tensor_size):
    def tensor_rank():
        if len(tensor_axes) == 1:
            return lax.axis_index(tensor_axes[0])
        return lax.axis_index(tensor_axes[0]) * tensor_size[1] + lax.axis_index(tensor_axes[1])

    def gather_rows(normed):
        rows = normed
        for name in tensor_axes:
            rows = lax.all_gather(rows, name, axis=1, tiled=True)
        return rows

    def to_gather_order(by_rank):
        s, w = by_rank.shape[1], by_rank.shape[2]
        if len(tensor_axes) == 1:
            return jnp.transpose(by_rank, (0, 2, 1)).reshape(-1)
        grid = by_rank.reshape(tensor_size[0], tensor_size[1], s, w)
        return jnp.transpose(grid, (1, 0, 3, 2)).reshape(-1)

    def from_gather_order(stats, s, w):
        k = stats.shape[0]
        if len(tensor_axes) == 1:
            return jnp.transpose(stats.reshape(k, tensor_size[0], w, s), (1, 0, 3, 2))
        grid = stats.reshape(k, tensor_size[1], tensor_size[0], w, s)
        grid = jnp.transpose(grid, (2, 1, 0, 4, 3))
        return grid.reshape(tensor_size[0] * tensor_size[1], k, s, w)

    def local(hidden, norm_gain, embedding, targets, lengths, loss_mask, deal_slots):
        group_rank = lax.axis_index("dp")
        sequences, row_width = hidden.shape[0], hidden.shape[1]
        ranks = int(np.prod(tensor_size))
        t_rank = tensor_rank()
        owned_seqs = group_rank * sequences + jnp.arange(sequences, dtype=jnp.int32)
        destination = deal_slots[owned_seqs] // sequences
        send_order = jnp.argsort(destination, stable=True)
        every_group = deal_slots // sequences
        arrived = jnp.argsort((every_group != group_rank).astype(jnp.int32), stable=True)[:sequences]
        arrived_slot = deal_slots[arrived] % sequences
        positions = t_rank * row_width + jnp.arange(row_width, dtype=jnp.int32)
        scored = (positions[None, :] < lengths[owned_seqs][:, None]) & (loss_mask == 1)
        marked = jnp.where(scored, targets, -1)
        undo_order = jnp.argsort(send_order)

        normed = normalize(hidden, norm_gain)
        row_block = gather_rows(normed)

        came = lax.all_to_all(marked[send_order], "dp", split_axis=0, concat_axis=0, tiled=True)
        worker_marks = came[jnp.argsort(arrived_slot)]
        spread = jnp.broadcast_to(worker_marks[None], (ranks,) + worker_marks.shape)
        block_marks = lax.all_to_all(spread, tensor_axes, split_axis=0, concat_axis=0, tiled=True)
        block_marks = to_gather_order(block_marks)

        offset = (t_rank * embedding.shape[0]).astype(jnp.int32)
        flat_rows = jnp.transpose(row_block, (1, 0, 2)).reshape(-1, row_block.shape[2])
        local_stats = row_stats(flat_rows, jnp.transpose(embedding), block_marks, offset)

        stats = from_gather_order(jnp.transpose(local_stats), sequences, row_width)
        parts = lax.all_to_all(stats, tensor_axes, split_axis=0, concat_axis=0, tiled=True)
        part_max, part_tot, part_wt, part_ch = parts[:, 0], parts[:, 1], parts[:, 2], parts[:, 3]
        overall = jnp.max(part_max, axis=0)
        factor = jnp.exp(part_max - overall[None])
        totals = jnp.sum(part_tot * factor, axis=0)
        weighted = jnp.sum(part_wt * factor, axis=0)
        chosen = jnp.sum(part_ch, axis=0)
        log_total = overall + jnp.log(totals)
        usable_rows = worker_marks >= 0
        log_prob = jnp.where(usable_rows, chosen - log_total, 0.0)
        entropy = jnp.where(usable_rows, log_total - weighted / totals, 0.0)

        both = jnp.stack([log_prob, entropy], axis=1)[arrived_slot]
        returned = lax.all_to_all(both, "dp", split_axis=0, concat_axis=0, tiled=True)[undo_order]
        return returned[:, 0], returned[:, 1]

    return local


PLANE = True
EMBEDDING_ROWS = 49664


def embedding_halves(mesh):
    rows = EMBEDDING_ROWS // mesh.shape["tensor"]
    return EMBEDDING_ROWS % mesh.shape["tensor"] == 0 and rows % 4 == 0


def split_dp(mesh):
    col = mesh.devices[:, 0]
    cores = len({getattr(d, "core_on_chip", 0) for d in col})
    if cores != 2 or col.size % cores:
        return None
    return col.size // cores, cores


def solution(mesh):
    split = split_tensor(mesh)
    cores = split_dp(mesh)
    if PLANE and split is not None and cores is not None and embedding_halves(mesh):
        sizes = (cores[0], cores[1], split[0], split[1])
        run_mesh = Mesh(mesh.devices.reshape(sizes), ("ty", "tc", "tx", "tz"))
        dp, tensor = ("ty", "tc"), ("tx", "tz")
        placed = (P(dp, tensor, None), P(), P(tensor, None), P(dp, tensor), P(), P(dp, tensor), P())
        return jax.shard_map(
            plane_fn(sizes), mesh=run_mesh, in_specs=placed,
            out_specs=(P(dp, tensor), P(dp, tensor)), check_vma=False,
        )
    if split is None:
        run_mesh, tensor_axes, tensor_size = mesh, ("tensor",), (mesh.shape["tensor"],)
    else:
        dp = mesh.shape["dp"]
        run_mesh = Mesh(mesh.devices.reshape(dp, split[0], split[1]), ("dp", "tx", "tz"))
        tensor_axes, tensor_size = ("tx", "tz"), split
    tensor = tensor_axes if len(tensor_axes) > 1 else tensor_axes[0]
    placed = (
        P("dp", tensor, None),
        P(),
        P(tensor, None),
        P("dp", tensor),
        P(),
        P("dp", tensor),
        P(),
    )
    return jax.shard_map(
        local_fn(tensor_axes, tensor_size),
        mesh=run_mesh,
        in_specs=placed,
        out_specs=(P("dp", tensor), P("dp", tensor)),
        check_vma=False,
    )
```

```python
import numpy as np
import jax
import jax.numpy as jnp
from jax import lax
from jax.experimental import pallas as pl
from jax.experimental.pallas import tpu as pltpu
from jax.sharding import Mesh
from jax.sharding import PartitionSpec as P

VREAL = 49155
INTERPRET = False
ROW_BLOCK = 512


def stats_kernel(offset_ref, rows_ref, emb_ref, marks_ref, out_ref):
    logits = jnp.dot(rows_ref[...], emb_ref[...], preferred_element_type=jnp.float32)
    columns = offset_ref[0] + lax.broadcasted_iota(jnp.int32, (1, logits.shape[1]), 1)
    bias = jnp.where(columns < VREAL, 0.0, -jnp.inf)
    masked = logits + bias
    maximum = jnp.max(masked, axis=1, keepdims=True)
    shift = jnp.maximum(maximum, jnp.finfo(jnp.float32).min)
    weights = jnp.exp(masked - shift)
    totals = jnp.sum(weights, axis=1, keepdims=True)
    weighted = jnp.sum(weights * logits, axis=1, keepdims=True)
    chosen = jnp.sum(jnp.where(columns == marks_ref[...], logits, 0.0), axis=1, keepdims=True)
    out_ref[...] = jnp.concatenate([maximum, totals, weighted, chosen], axis=1)


def row_stats(rows, emb_t, marks, offset):
    n, d = rows.shape
    v = emb_t.shape[1]
    block = ROW_BLOCK if n % ROW_BLOCK == 0 else n
    return pl.pallas_call(
        stats_kernel,
        grid=(n // block,),
        in_specs=[
            pl.BlockSpec(memory_space=pltpu.SMEM),
            pl.BlockSpec((block, d), lambda i: (i, 0)),
            pl.BlockSpec((d, v), lambda i: (0, 0)),
            pl.BlockSpec((block, 1), lambda i: (i, 0)),
        ],
        out_specs=pl.BlockSpec((block, 4), lambda i: (i, 0)),
        out_shape=jax.ShapeDtypeStruct((n, 4), jnp.float32),
        cost_estimate=pl.CostEstimate(
            flops=2 * n * v * d, transcendentals=n * v, bytes_accessed=2 * (n + v) * d + 20 * n
        ),
        interpret=INTERPRET,
    )(offset.reshape(1), rows, emb_t, marks.reshape(n, 1))


def normalize(hidden, norm_gain):
    values = hidden.astype(jnp.float32)
    inverse = lax.rsqrt(jnp.mean(values * values, axis=2, keepdims=True) + 1e-05)
    return (values * inverse * norm_gain).astype(jnp.bfloat16)


def split_tensor(mesh):
    row = mesh.devices[0]
    slow = len({tuple(d.coords)[0] for d in row})
    if row.size % slow or slow in (1, row.size):
        return None
    return slow, row.size // slow


def local_fn(tensor_axes, tensor_size):
    def tensor_rank():
        if len(tensor_axes) == 1:
            return lax.axis_index(tensor_axes[0])
        return lax.axis_index(tensor_axes[0]) * tensor_size[1] + lax.axis_index(tensor_axes[1])

    def gather_rows(normed):
        rows = normed
        for name in tensor_axes:
            rows = lax.all_gather(rows, name, axis=1, tiled=True)
        return rows

    def to_gather_order(by_rank):
        s, w = by_rank.shape[1], by_rank.shape[2]
        if len(tensor_axes) == 1:
            return jnp.transpose(by_rank, (0, 2, 1)).reshape(-1)
        grid = by_rank.reshape(tensor_size[0], tensor_size[1], s, w)
        return jnp.transpose(grid, (1, 0, 3, 2)).reshape(-1)

    def from_gather_order(stats, s, w):
        k = stats.shape[0]
        if len(tensor_axes) == 1:
            return jnp.transpose(stats.reshape(k, tensor_size[0], w, s), (1, 0, 3, 2))
        grid = stats.reshape(k, tensor_size[1], tensor_size[0], w, s)
        grid = jnp.transpose(grid, (2, 1, 0, 4, 3))
        return grid.reshape(tensor_size[0] * tensor_size[1], k, s, w)

    def local(hidden, norm_gain, embedding, targets, lengths, loss_mask, deal_slots):
        group_rank = lax.axis_index("dp")
        sequences, row_width = hidden.shape[0], hidden.shape[1]
        ranks = int(np.prod(tensor_size))
        t_rank = tensor_rank()
        owned_seqs = group_rank * sequences + jnp.arange(sequences, dtype=jnp.int32)
        destination = deal_slots[owned_seqs] // sequences
        send_order = jnp.argsort(destination, stable=True)
        every_group = deal_slots // sequences
        arrived = jnp.argsort((every_group != group_rank).astype(jnp.int32), stable=True)[:sequences]
        arrived_slot = deal_slots[arrived] % sequences
        positions = t_rank * row_width + jnp.arange(row_width, dtype=jnp.int32)
        scored = (positions[None, :] < lengths[owned_seqs][:, None]) & (loss_mask == 1)
        marked = jnp.where(scored, targets, -1)
        undo_order = jnp.argsort(send_order)

        normed = normalize(hidden, norm_gain)
        row_block = gather_rows(normed)

        came = lax.all_to_all(marked[send_order], "dp", split_axis=0, concat_axis=0, tiled=True)
        worker_marks = came[jnp.argsort(arrived_slot)]
        spread = jnp.broadcast_to(worker_marks[None], (ranks,) + worker_marks.shape)
        block_marks = lax.all_to_all(spread, tensor_axes, split_axis=0, concat_axis=0, tiled=True)
        block_marks = to_gather_order(block_marks)

        offset = (t_rank * embedding.shape[0]).astype(jnp.int32)
        flat_rows = jnp.transpose(row_block, (1, 0, 2)).reshape(-1, row_block.shape[2])
        local_stats = row_stats(flat_rows, jnp.transpose(embedding), block_marks, offset)

        stats = from_gather_order(jnp.transpose(local_stats), sequences, row_width)
        parts = lax.all_to_all(stats, tensor_axes, split_axis=0, concat_axis=0, tiled=True)
        part_max, part_tot, part_wt, part_ch = parts[:, 0], parts[:, 1], parts[:, 2], parts[:, 3]
        overall = jnp.max(part_max, axis=0)
        factor = jnp.exp(part_max - overall[None])
        totals = jnp.sum(part_tot * factor, axis=0)
        weighted = jnp.sum(part_wt * factor, axis=0)
        chosen = jnp.sum(part_ch, axis=0)
        log_total = overall + jnp.log(totals)
        usable_rows = worker_marks >= 0
        log_prob = jnp.where(usable_rows, chosen - log_total, 0.0)
        entropy = jnp.where(usable_rows, log_total - weighted / totals, 0.0)

        both = jnp.stack([log_prob, entropy], axis=1)[arrived_slot]
        returned = lax.all_to_all(both, "dp", split_axis=0, concat_axis=0, tiled=True)[undo_order]
        return returned[:, 0], returned[:, 1]

    return local


def solution(mesh):
    split = split_tensor(mesh)
    if split is None:
        run_mesh, tensor_axes, tensor_size = mesh, ("tensor",), (mesh.shape["tensor"],)
    else:
        dp = mesh.shape["dp"]
        run_mesh = Mesh(mesh.devices.reshape(dp, split[0], split[1]), ("dp", "tx", "tz"))
        tensor_axes, tensor_size = ("tx", "tz"), split
    tensor = tensor_axes if len(tensor_axes) > 1 else tensor_axes[0]
    placed = (
        P("dp", tensor, None),
        P(),
        P(tensor, None),
        P("dp", tensor),
        P(),
        P("dp", tensor),
        P(),
    )
    return jax.shard_map(
        local_fn(tensor_axes, tensor_size),
        mesh=run_mesh,
        in_specs=placed,
        out_specs=(P("dp", tensor), P("dp", tensor)),
        check_vma=False,
    )
```

```python
import numpy as np
import jax
import jax.numpy as jnp
from jax import lax
from jax.experimental import pallas as pl
from jax.experimental.pallas import tpu as pltpu
from jax.sharding import Mesh
from jax.sharding import PartitionSpec as P

VREAL = 49155
INTERPRET = False
ROW_BLOCK = 512


def stats_kernel(offset_ref, rows_ref, emb_ref, marks_ref, out_ref):
    logits = jnp.dot(rows_ref[...], emb_ref[...], preferred_element_type=jnp.float32)
    columns = offset_ref[0] + lax.broadcasted_iota(jnp.int32, (1, logits.shape[1]), 1)
    bias = jnp.where(columns < VREAL, 0.0, -jnp.inf)
    masked = logits + bias
    maximum = jnp.max(masked, axis=1, keepdims=True)
    shift = jnp.maximum(maximum, jnp.finfo(jnp.float32).min)
    weights = jnp.exp(masked - shift)
    totals = jnp.sum(weights, axis=1, keepdims=True)
    weighted = jnp.sum(weights * logits, axis=1, keepdims=True)
    chosen = jnp.sum(jnp.where(columns == marks_ref[...], logits, 0.0), axis=1, keepdims=True)
    out_ref[...] = jnp.concatenate([maximum, totals, weighted, chosen], axis=1)


def row_stats(rows, emb_t, marks, offset):
    n, d = rows.shape
    v = emb_t.shape[1]
    block = ROW_BLOCK if n % ROW_BLOCK == 0 else n
    return pl.pallas_call(
        stats_kernel,
        grid=(n // block,),
        in_specs=[
            pl.BlockSpec(memory_space=pltpu.SMEM),
            pl.BlockSpec((block, d), lambda i: (i, 0)),
            pl.BlockSpec((d, v), lambda i: (0, 0)),
            pl.BlockSpec((block, 1), lambda i: (i, 0)),
        ],
        out_specs=pl.BlockSpec((block, 4), lambda i: (i, 0)),
        out_shape=jax.ShapeDtypeStruct((n, 4), jnp.float32),
        cost_estimate=pl.CostEstimate(
            flops=2 * n * v * d, transcendentals=n * v, bytes_accessed=2 * (n + v) * d + 20 * n
        ),
        interpret=INTERPRET,
    )(offset.reshape(1), rows, emb_t, marks.reshape(n, 1))


def normalize(hidden, norm_gain):
    values = hidden.astype(jnp.float32)
    inverse = lax.rsqrt(jnp.mean(values * values, axis=2, keepdims=True) + 1e-05)
    return (values * inverse * norm_gain).astype(jnp.bfloat16)


def split_tensor(mesh):
    row = mesh.devices[0]
    slow = len({tuple(d.coords)[0] for d in row})
    if row.size % slow or slow in (1, row.size):
        return None
    return slow, row.size // slow


def local_fn(tensor_axes, tensor_size):
    def tensor_rank():
        if len(tensor_axes) == 1:
            return lax.axis_index(tensor_axes[0])
        return lax.axis_index(tensor_axes[0]) * tensor_size[1] + lax.axis_index(tensor_axes[1])

    def gather_rows(normed):
        rows = normed
        for i, name in enumerate(tensor_axes):
            if i == 0 and len(tensor_axes) > 1:
                spread = jnp.broadcast_to(rows[None], (tensor_size[0],) + rows.shape)
                got = lax.all_to_all(spread, name, split_axis=0, concat_axis=0, tiled=True)
                rows = jnp.transpose(got, (1, 0, 2, 3)).reshape(rows.shape[0], -1, rows.shape[2])
            else:
                rows = lax.all_gather(rows, name, axis=1, tiled=True)
        return rows

    def to_gather_order(by_rank):
        s, w = by_rank.shape[1], by_rank.shape[2]
        if len(tensor_axes) == 1:
            return jnp.transpose(by_rank, (0, 2, 1)).reshape(-1)
        grid = by_rank.reshape(tensor_size[0], tensor_size[1], s, w)
        return jnp.transpose(grid, (1, 0, 3, 2)).reshape(-1)

    def from_gather_order(stats, s, w):
        k = stats.shape[0]
        if len(tensor_axes) == 1:
            return jnp.transpose(stats.reshape(k, tensor_size[0], w, s), (1, 0, 3, 2))
        grid = stats.reshape(k, tensor_size[1], tensor_size[0], w, s)
        grid = jnp.transpose(grid, (2, 1, 0, 4, 3))
        return grid.reshape(tensor_size[0] * tensor_size[1], k, s, w)

    def local(hidden, norm_gain, embedding, targets, lengths, loss_mask, deal_slots):
        group_rank = lax.axis_index("dp")
        sequences, row_width = hidden.shape[0], hidden.shape[1]
        ranks = int(np.prod(tensor_size))
        t_rank = tensor_rank()
        owned_seqs = group_rank * sequences + jnp.arange(sequences, dtype=jnp.int32)
        destination = deal_slots[owned_seqs] // sequences
        send_order = jnp.argsort(destination, stable=True)
        every_group = deal_slots // sequences
        arrived = jnp.argsort((every_group != group_rank).astype(jnp.int32), stable=True)[:sequences]
        arrived_slot = deal_slots[arrived] % sequences
        positions = t_rank * row_width + jnp.arange(row_width, dtype=jnp.int32)
        scored = (positions[None, :] < lengths[owned_seqs][:, None]) & (loss_mask == 1)
        marked = jnp.where(scored, targets, -1)
        undo_order = jnp.argsort(send_order)

        normed = normalize(hidden, norm_gain)
        row_block = gather_rows(normed)

        came = lax.all_to_all(marked[send_order], "dp", split_axis=0, concat_axis=0, tiled=True)
        worker_marks = came[jnp.argsort(arrived_slot)]
        spread = jnp.broadcast_to(worker_marks[None], (ranks,) + worker_marks.shape)
        block_marks = lax.all_to_all(spread, tensor_axes, split_axis=0, concat_axis=0, tiled=True)
        block_marks = to_gather_order(block_marks)

        offset = (t_rank * embedding.shape[0]).astype(jnp.int32)
        flat_rows = jnp.transpose(row_block, (1, 0, 2)).reshape(-1, row_block.shape[2])
        local_stats = row_stats(flat_rows, jnp.transpose(embedding), block_marks, offset)

        stats = from_gather_order(jnp.transpose(local_stats), sequences, row_width)
        parts = lax.all_to_all(stats, tensor_axes, split_axis=0, concat_axis=0, tiled=True)
        part_max, part_tot, part_wt, part_ch = parts[:, 0], parts[:, 1], parts[:, 2], parts[:, 3]
        overall = jnp.max(part_max, axis=0)
        factor = jnp.exp(part_max - overall[None])
        totals = jnp.sum(part_tot * factor, axis=0)
        weighted = jnp.sum(part_wt * factor, axis=0)
        chosen = jnp.sum(part_ch, axis=0)
        log_total = overall + jnp.log(totals)
        usable_rows = worker_marks >= 0
        log_prob = jnp.where(usable_rows, chosen - log_total, 0.0)
        entropy = jnp.where(usable_rows, log_total - weighted / totals, 0.0)

        both = jnp.stack([log_prob, entropy], axis=1)[arrived_slot]
        returned = lax.all_to_all(both, "dp", split_axis=0, concat_axis=0, tiled=True)[undo_order]
        return returned[:, 0], returned[:, 1]

    return local


def solution(mesh):
    split = split_tensor(mesh)
    if split is None:
        run_mesh, tensor_axes, tensor_size = mesh, ("tensor",), (mesh.shape["tensor"],)
    else:
        dp = mesh.shape["dp"]
        run_mesh = Mesh(mesh.devices.reshape(dp, split[0], split[1]), ("dp", "tx", "tz"))
        tensor_axes, tensor_size = ("tx", "tz"), split
    tensor = tensor_axes if len(tensor_axes) > 1 else tensor_axes[0]
    placed = (
        P("dp", tensor, None),
        P(),
        P(tensor, None),
        P("dp", tensor),
        P(),
        P("dp", tensor),
        P(),
    )
    return jax.shard_map(
        local_fn(tensor_axes, tensor_size),
        mesh=run_mesh,
        in_specs=placed,
        out_specs=(P("dp", tensor), P("dp", tensor)),
        check_vma=False,
    )
```

```python
import numpy as np
import jax
import jax.numpy as jnp
from jax import lax
from jax.experimental import pallas as pl
from jax.experimental.pallas import tpu as pltpu
from jax.sharding import Mesh
from jax.sharding import PartitionSpec as P

VREAL = 49155
INTERPRET = False
ROW_BLOCK = 512


def stats_kernel(offset_ref, rows_ref, emb_ref, marks_ref, out_ref):
    logits = jnp.dot(rows_ref[...], emb_ref[...], preferred_element_type=jnp.float32)
    columns = offset_ref[0] + lax.broadcasted_iota(jnp.int32, (1, logits.shape[1]), 1)
    bias = jnp.where(columns < VREAL, 0.0, -jnp.inf)
    masked = logits + bias
    maximum = jnp.max(masked, axis=1, keepdims=True)
    shift = jnp.maximum(maximum, jnp.finfo(jnp.float32).min)
    weights = jnp.exp(masked - shift)
    totals = jnp.sum(weights, axis=1, keepdims=True)
    weighted = jnp.sum(weights * logits, axis=1, keepdims=True)
    chosen = jnp.sum(jnp.where(columns == marks_ref[...], logits, 0.0), axis=1, keepdims=True)
    out_ref[...] = jnp.concatenate([maximum, totals, weighted, chosen], axis=1)


def row_stats(rows, emb_t, marks, offset):
    n, d = rows.shape
    v = emb_t.shape[1]
    block = ROW_BLOCK if n % ROW_BLOCK == 0 else n
    return pl.pallas_call(
        stats_kernel,
        grid=(n // block,),
        in_specs=[
            pl.BlockSpec(memory_space=pltpu.SMEM),
            pl.BlockSpec((block, d), lambda i: (i, 0)),
            pl.BlockSpec((d, v), lambda i: (0, 0)),
            pl.BlockSpec((block, 1), lambda i: (i, 0)),
        ],
        out_specs=pl.BlockSpec((block, 4), lambda i: (i, 0)),
        out_shape=jax.ShapeDtypeStruct((n, 4), jnp.float32),
        cost_estimate=pl.CostEstimate(
            flops=2 * n * v * d, transcendentals=n * v, bytes_accessed=2 * (n + v) * d + 20 * n
        ),
        interpret=INTERPRET,
    )(offset.reshape(1), rows, emb_t, marks.reshape(n, 1))


def normalize(hidden, norm_gain):
    values = hidden.astype(jnp.float32)
    inverse = lax.rsqrt(jnp.mean(values * values, axis=2, keepdims=True) + 1e-05)
    return (values * inverse * norm_gain).astype(jnp.bfloat16)


def split_tensor(mesh):
    row = mesh.devices[0]
    slow = len({tuple(d.coords)[0] for d in row})
    if row.size % slow or slow in (1, row.size):
        return None
    return slow, row.size // slow


def local_fn(tensor_axes, tensor_size, dp_size):
    def tensor_rank():
        if len(tensor_axes) == 1:
            return lax.axis_index(tensor_axes[0])
        return lax.axis_index(tensor_axes[0]) * tensor_size[1] + lax.axis_index(tensor_axes[1])

    def gather_rows(normed):
        rows = normed
        for i, name in enumerate(tensor_axes):
            if i == 0 and len(tensor_axes) > 1:
                spread = jnp.broadcast_to(rows[None], (tensor_size[0],) + rows.shape)
                got = lax.all_to_all(spread, name, split_axis=0, concat_axis=0, tiled=True)
                rows = jnp.transpose(got, (1, 0, 2, 3)).reshape(rows.shape[0], -1, rows.shape[2])
            else:
                rows = lax.all_gather(rows, name, axis=1, tiled=True)
        return rows

    def to_gather_order(by_rank):
        s, w = by_rank.shape[1], by_rank.shape[2]
        if len(tensor_axes) == 1:
            return jnp.transpose(by_rank, (0, 2, 1)).reshape(-1)
        grid = by_rank.reshape(tensor_size[0], tensor_size[1], s, w)
        return jnp.transpose(grid, (1, 0, 3, 2)).reshape(-1)

    def from_gather_order(stats, s, w):
        k = stats.shape[0]
        if len(tensor_axes) == 1:
            return jnp.transpose(stats.reshape(k, tensor_size[0], w, s), (1, 0, 3, 2))
        grid = stats.reshape(k, tensor_size[1], tensor_size[0], w, s)
        grid = jnp.transpose(grid, (2, 1, 0, 4, 3))
        return grid.reshape(tensor_size[0] * tensor_size[1], k, s, w)

    def exchange(chunks, group_rank):
        groups = chunks.shape[0] // (chunks.shape[0] // dp_size)
        per = chunks.shape[0] // groups
        blocks = chunks.reshape((groups, per) + chunks.shape[1:])
        got = []
        for shift in range(groups):
            send = jnp.take(blocks, (group_rank + shift) % groups, axis=0)
            if shift:
                send = lax.ppermute(send, "dp", [(i, (i + shift) % groups) for i in range(groups)])
            got.append(send)
        order = (group_rank - jnp.arange(groups)) % groups
        by_source = jnp.stack(got)[jnp.argsort(order)]
        return by_source.reshape(chunks.shape)

    def local(hidden, norm_gain, embedding, targets, lengths, loss_mask, deal_slots):
        group_rank = lax.axis_index("dp")
        sequences, row_width = hidden.shape[0], hidden.shape[1]
        ranks = int(np.prod(tensor_size))
        t_rank = tensor_rank()
        owned_seqs = group_rank * sequences + jnp.arange(sequences, dtype=jnp.int32)
        destination = deal_slots[owned_seqs] // sequences
        send_order = jnp.argsort(destination, stable=True)
        every_group = deal_slots // sequences
        arrived = jnp.argsort((every_group != group_rank).astype(jnp.int32), stable=True)[:sequences]
        arrived_slot = deal_slots[arrived] % sequences
        positions = t_rank * row_width + jnp.arange(row_width, dtype=jnp.int32)
        scored = (positions[None, :] < lengths[owned_seqs][:, None]) & (loss_mask == 1)
        marked = jnp.where(scored, targets, -1)
        undo_order = jnp.argsort(send_order)

        normed = normalize(hidden, norm_gain)
        row_block = gather_rows(normed)

        came = lax.all_to_all(marked[send_order], "dp", split_axis=0, concat_axis=0, tiled=True)
        worker_marks = came[jnp.argsort(arrived_slot)]
        spread = jnp.broadcast_to(worker_marks[None], (ranks,) + worker_marks.shape)
        block_marks = lax.all_to_all(spread, tensor_axes, split_axis=0, concat_axis=0, tiled=True)
        block_marks = to_gather_order(block_marks)

        offset = (t_rank * embedding.shape[0]).astype(jnp.int32)
        flat_rows = jnp.transpose(row_block, (1, 0, 2)).reshape(-1, row_block.shape[2])
        local_stats = row_stats(flat_rows, jnp.transpose(embedding), block_marks, offset)

        stats = from_gather_order(jnp.transpose(local_stats), sequences, row_width)
        parts = lax.all_to_all(stats, tensor_axes, split_axis=0, concat_axis=0, tiled=True)
        part_max, part_tot, part_wt, part_ch = parts[:, 0], parts[:, 1], parts[:, 2], parts[:, 3]
        overall = jnp.max(part_max, axis=0)
        factor = jnp.exp(part_max - overall[None])
        totals = jnp.sum(part_tot * factor, axis=0)
        weighted = jnp.sum(part_wt * factor, axis=0)
        chosen = jnp.sum(part_ch, axis=0)
        log_total = overall + jnp.log(totals)
        usable_rows = worker_marks >= 0
        log_prob = jnp.where(usable_rows, chosen - log_total, 0.0)
        entropy = jnp.where(usable_rows, log_total - weighted / totals, 0.0)

        both = jnp.stack([log_prob, entropy], axis=1)[arrived_slot]
        returned = exchange(both, group_rank)[undo_order]
        return returned[:, 0], returned[:, 1]

    return local


def solution(mesh):
    split = split_tensor(mesh)
    if split is None:
        run_mesh, tensor_axes, tensor_size = mesh, ("tensor",), (mesh.shape["tensor"],)
    else:
        dp = mesh.shape["dp"]
        run_mesh = Mesh(mesh.devices.reshape(dp, split[0], split[1]), ("dp", "tx", "tz"))
        tensor_axes, tensor_size = ("tx", "tz"), split
    tensor = tensor_axes if len(tensor_axes) > 1 else tensor_axes[0]
    placed = (
        P("dp", tensor, None),
        P(),
        P(tensor, None),
        P("dp", tensor),
        P(),
        P("dp", tensor),
        P(),
    )
    return jax.shard_map(
        local_fn(tensor_axes, tensor_size, mesh.shape["dp"]),
        mesh=run_mesh,
        in_specs=placed,
        out_specs=(P("dp", tensor), P("dp", tensor)),
        check_vma=False,
    )
```

```python
import numpy as np
import jax
import jax.numpy as jnp
from jax import lax
from jax.experimental import pallas as pl
from jax.experimental.pallas import tpu as pltpu
from jax.sharding import Mesh
from jax.sharding import PartitionSpec as P

VREAL = 49155
INTERPRET = False
ROW_BLOCK = 512


def stats_kernel(offset_ref, emb_ref, rows_ref, marks_ref, out_ref):
    logits = lax.dot_general(
        emb_ref[...], rows_ref[...], (((1,), (1,)), ((), ())), preferred_element_type=jnp.float32
    )
    columns = offset_ref[0] + lax.broadcasted_iota(jnp.int32, (logits.shape[0], 1), 0)
    bias = jnp.where(columns < VREAL, 0.0, -jnp.inf)
    masked = logits + bias
    maximum = jnp.max(masked, axis=0, keepdims=True)
    shift = jnp.maximum(maximum, jnp.finfo(jnp.float32).min)
    weights = jnp.exp(masked - shift)
    totals = jnp.sum(weights, axis=0, keepdims=True)
    weighted = jnp.sum(weights * logits, axis=0, keepdims=True)
    chosen = jnp.sum(jnp.where(columns == marks_ref[...], logits, 0.0), axis=0, keepdims=True)
    out_ref[...] = jnp.concatenate([maximum, totals, weighted, chosen], axis=0)


def row_stats(rows, embedding, marks, offset):
    n, d = rows.shape
    v = embedding.shape[0]
    block = ROW_BLOCK if n % ROW_BLOCK == 0 else n
    return pl.pallas_call(
        stats_kernel,
        grid=(n // block,),
        in_specs=[
            pl.BlockSpec(memory_space=pltpu.SMEM),
            pl.BlockSpec((v, d), lambda i: (0, 0)),
            pl.BlockSpec((block, d), lambda i: (i, 0)),
            pl.BlockSpec((1, block), lambda i: (0, i)),
        ],
        out_specs=pl.BlockSpec((4, block), lambda i: (0, i)),
        out_shape=jax.ShapeDtypeStruct((4, n), jnp.float32),
        cost_estimate=pl.CostEstimate(
            flops=2 * n * v * d, transcendentals=n * v, bytes_accessed=2 * (n + v) * d + 20 * n
        ),
        interpret=INTERPRET,
    )(offset.reshape(1), embedding, rows, marks.reshape(1, n))


def normalize(hidden, norm_gain):
    values = hidden.astype(jnp.float32)
    inverse = lax.rsqrt(jnp.mean(values * values, axis=2, keepdims=True) + 1e-05)
    return (values * inverse * norm_gain).astype(jnp.bfloat16)


def split_tensor(mesh):
    row = mesh.devices[0]
    slow = len({tuple(d.coords)[0] for d in row})
    if row.size % slow or slow in (1, row.size):
        return None
    return slow, row.size // slow


def local_fn(tensor_axes, tensor_size):
    def tensor_rank():
        if len(tensor_axes) == 1:
            return lax.axis_index(tensor_axes[0])
        return lax.axis_index(tensor_axes[0]) * tensor_size[1] + lax.axis_index(tensor_axes[1])

    def gather_rows(normed):
        rows = normed
        for i, name in enumerate(tensor_axes):
            if i == 0 and len(tensor_axes) > 1:
                spread = jnp.broadcast_to(rows[None], (tensor_size[0],) + rows.shape)
                got = lax.all_to_all(spread, name, split_axis=0, concat_axis=0, tiled=True)
                rows = jnp.transpose(got, (1, 0, 2, 3)).reshape(rows.shape[0], -1, rows.shape[2])
            else:
                rows = lax.all_gather(rows, name, axis=1, tiled=True)
        return rows

    def to_gather_order(by_rank):
        s, w = by_rank.shape[1], by_rank.shape[2]
        if len(tensor_axes) == 1:
            return jnp.transpose(by_rank, (0, 2, 1)).reshape(-1)
        grid = by_rank.reshape(tensor_size[0], tensor_size[1], s, w)
        return jnp.transpose(grid, (1, 0, 3, 2)).reshape(-1)

    def from_gather_order(stats, s, w):
        k = stats.shape[0]
        if len(tensor_axes) == 1:
            return jnp.transpose(stats.reshape(k, tensor_size[0], w, s), (1, 0, 3, 2))
        grid = stats.reshape(k, tensor_size[1], tensor_size[0], w, s)
        grid = jnp.transpose(grid, (2, 1, 0, 4, 3))
        return grid.reshape(tensor_size[0] * tensor_size[1], k, s, w)

    def local(hidden, norm_gain, embedding, targets, lengths, loss_mask, deal_slots):
        group_rank = lax.axis_index("dp")
        sequences, row_width = hidden.shape[0], hidden.shape[1]
        ranks = int(np.prod(tensor_size))
        t_rank = tensor_rank()
        owned_seqs = group_rank * sequences + jnp.arange(sequences, dtype=jnp.int32)
        destination = deal_slots[owned_seqs] // sequences
        send_order = jnp.argsort(destination, stable=True)
        every_group = deal_slots // sequences
        arrived = jnp.argsort((every_group != group_rank).astype(jnp.int32), stable=True)[:sequences]
        arrived_slot = deal_slots[arrived] % sequences
        positions = t_rank * row_width + jnp.arange(row_width, dtype=jnp.int32)
        scored = (positions[None, :] < lengths[owned_seqs][:, None]) & (loss_mask == 1)
        marked = jnp.where(scored, targets, -1)
        undo_order = jnp.argsort(send_order)

        normed = normalize(hidden, norm_gain)
        row_block = gather_rows(normed)

        came = lax.all_to_all(marked[send_order], "dp", split_axis=0, concat_axis=0, tiled=True)
        worker_marks = came[jnp.argsort(arrived_slot)]
        spread = jnp.broadcast_to(worker_marks[None], (ranks,) + worker_marks.shape)
        block_marks = lax.all_to_all(spread, tensor_axes, split_axis=0, concat_axis=0, tiled=True)
        block_marks = to_gather_order(block_marks)

        offset = (t_rank * embedding.shape[0]).astype(jnp.int32)
        flat_rows = jnp.transpose(row_block, (1, 0, 2)).reshape(-1, row_block.shape[2])
        local_stats = row_stats(flat_rows, embedding, block_marks, offset)

        stats = from_gather_order(local_stats, sequences, row_width)
        parts = lax.all_to_all(stats, tensor_axes, split_axis=0, concat_axis=0, tiled=True)
        part_max, part_tot, part_wt, part_ch = parts[:, 0], parts[:, 1], parts[:, 2], parts[:, 3]
        overall = jnp.max(part_max, axis=0)
        factor = jnp.exp(part_max - overall[None])
        totals = jnp.sum(part_tot * factor, axis=0)
        weighted = jnp.sum(part_wt * factor, axis=0)
        chosen = jnp.sum(part_ch, axis=0)
        log_total = overall + jnp.log(totals)
        usable_rows = worker_marks >= 0
        log_prob = jnp.where(usable_rows, chosen - log_total, 0.0)
        entropy = jnp.where(usable_rows, log_total - weighted / totals, 0.0)

        both = jnp.stack([log_prob, entropy], axis=1)[arrived_slot]
        returned = lax.all_to_all(both, "dp", split_axis=0, concat_axis=0, tiled=True)[undo_order]
        return returned[:, 0], returned[:, 1]

    return local


def solution(mesh):
    split = split_tensor(mesh)
    if split is None:
        run_mesh, tensor_axes, tensor_size = mesh, ("tensor",), (mesh.shape["tensor"],)
    else:
        dp = mesh.shape["dp"]
        run_mesh = Mesh(mesh.devices.reshape(dp, split[0], split[1]), ("dp", "tx", "tz"))
        tensor_axes, tensor_size = ("tx", "tz"), split
    tensor = tensor_axes if len(tensor_axes) > 1 else tensor_axes[0]
    placed = (
        P("dp", tensor, None),
        P(),
        P(tensor, None),
        P("dp", tensor),
        P(),
        P("dp", tensor),
        P(),
    )
    return jax.shard_map(
        local_fn(tensor_axes, tensor_size),
        mesh=run_mesh,
        in_specs=placed,
        out_specs=(P("dp", tensor), P("dp", tensor)),
        check_vma=False,
    )
```

```python
import numpy as np
import jax
import jax.numpy as jnp
from jax import lax
from jax.experimental import pallas as pl
from jax.experimental.pallas import tpu as pltpu
from jax.sharding import Mesh
from jax.sharding import PartitionSpec as P

VREAL = 49155
INTERPRET = False
ROW_BLOCK = 1024


def stats_kernel(offset_ref, emb_ref, rows_ref, marks_ref, out_ref):
    logits = lax.dot_general(
        emb_ref[...], rows_ref[...], (((1,), (1,)), ((), ())), preferred_element_type=jnp.float32
    )
    columns = offset_ref[0] + lax.broadcasted_iota(jnp.int32, (logits.shape[0], 1), 0)
    bias = jnp.where(columns < VREAL, 0.0, -jnp.inf)
    masked = logits + bias
    maximum = jnp.max(masked, axis=0, keepdims=True)
    shift = jnp.maximum(maximum, jnp.finfo(jnp.float32).min)
    weights = jnp.exp(masked - shift)
    totals = jnp.sum(weights, axis=0, keepdims=True)
    weighted = jnp.sum(weights * logits, axis=0, keepdims=True)
    chosen = jnp.sum(jnp.where(columns == marks_ref[...], logits, 0.0), axis=0, keepdims=True)
    out_ref[...] = jnp.concatenate([maximum, totals, weighted, chosen], axis=0)


def row_stats(rows, embedding, marks, offset):
    n, d = rows.shape
    v = embedding.shape[0]
    block = ROW_BLOCK if n % ROW_BLOCK == 0 else n
    return pl.pallas_call(
        stats_kernel,
        grid=(n // block,),
        in_specs=[
            pl.BlockSpec(memory_space=pltpu.SMEM),
            pl.BlockSpec((v, d), lambda i: (0, 0)),
            pl.BlockSpec((block, d), lambda i: (i, 0)),
            pl.BlockSpec((1, block), lambda i: (0, i)),
        ],
        out_specs=pl.BlockSpec((4, block), lambda i: (0, i)),
        out_shape=jax.ShapeDtypeStruct((4, n), jnp.float32),
        cost_estimate=pl.CostEstimate(
            flops=2 * n * v * d, transcendentals=n * v, bytes_accessed=2 * (n + v) * d + 20 * n
        ),
        interpret=INTERPRET,
    )(offset.reshape(1), embedding, rows, marks.reshape(1, n))


def normalize(hidden, norm_gain):
    values = hidden.astype(jnp.float32)
    inverse = lax.rsqrt(jnp.mean(values * values, axis=2, keepdims=True) + 1e-05)
    return (values * inverse * norm_gain).astype(jnp.bfloat16)


def split_tensor(mesh):
    row = mesh.devices[0]
    slow = len({tuple(d.coords)[0] for d in row})
    if row.size % slow or slow in (1, row.size):
        return None
    return slow, row.size // slow


def local_fn(tensor_axes, tensor_size):
    def tensor_rank():
        if len(tensor_axes) == 1:
            return lax.axis_index(tensor_axes[0])
        return lax.axis_index(tensor_axes[0]) * tensor_size[1] + lax.axis_index(tensor_axes[1])

    def gather_rows(normed):
        rows = normed
        for i, name in enumerate(tensor_axes):
            if i == 0 and len(tensor_axes) > 1:
                spread = jnp.broadcast_to(rows[None], (tensor_size[0],) + rows.shape)
                got = lax.all_to_all(spread, name, split_axis=0, concat_axis=0, tiled=True)
                rows = jnp.transpose(got, (1, 0, 2, 3)).reshape(rows.shape[0], -1, rows.shape[2])
            else:
                rows = lax.all_gather(rows, name, axis=1, tiled=True)
        return rows

    def to_gather_order(by_rank):
        s, w = by_rank.shape[1], by_rank.shape[2]
        if len(tensor_axes) == 1:
            return jnp.transpose(by_rank, (0, 2, 1)).reshape(-1)
        grid = by_rank.reshape(tensor_size[0], tensor_size[1], s, w)
        return jnp.transpose(grid, (1, 0, 3, 2)).reshape(-1)

    def from_gather_order(stats, s, w):
        k = stats.shape[0]
        if len(tensor_axes) == 1:
            return jnp.transpose(stats.reshape(k, tensor_size[0], w, s), (1, 0, 3, 2))
        grid = stats.reshape(k, tensor_size[1], tensor_size[0], w, s)
        grid = jnp.transpose(grid, (2, 1, 0, 4, 3))
        return grid.reshape(tensor_size[0] * tensor_size[1], k, s, w)

    def local(hidden, norm_gain, embedding, targets, lengths, loss_mask, deal_slots):
        group_rank = lax.axis_index("dp")
        sequences, row_width = hidden.shape[0], hidden.shape[1]
        ranks = int(np.prod(tensor_size))
        t_rank = tensor_rank()
        owned_seqs = group_rank * sequences + jnp.arange(sequences, dtype=jnp.int32)
        destination = deal_slots[owned_seqs] // sequences
        send_order = jnp.argsort(destination, stable=True)
        every_group = deal_slots // sequences
        arrived = jnp.argsort((every_group != group_rank).astype(jnp.int32), stable=True)[:sequences]
        arrived_slot = deal_slots[arrived] % sequences
        positions = t_rank * row_width + jnp.arange(row_width, dtype=jnp.int32)
        scored = (positions[None, :] < lengths[owned_seqs][:, None]) & (loss_mask == 1)
        marked = jnp.where(scored, targets, -1)
        undo_order = jnp.argsort(send_order)

        normed = normalize(hidden, norm_gain)
        row_block = gather_rows(normed)

        came = lax.all_to_all(marked[send_order], "dp", split_axis=0, concat_axis=0, tiled=True)
        worker_marks = came[jnp.argsort(arrived_slot)]
        spread = jnp.broadcast_to(worker_marks[None], (ranks,) + worker_marks.shape)
        block_marks = lax.all_to_all(spread, tensor_axes, split_axis=0, concat_axis=0, tiled=True)
        block_marks = to_gather_order(block_marks)

        offset = (t_rank * embedding.shape[0]).astype(jnp.int32)
        flat_rows = jnp.transpose(row_block, (1, 0, 2)).reshape(-1, row_block.shape[2])
        local_stats = row_stats(flat_rows, embedding, block_marks, offset)

        stats = from_gather_order(local_stats, sequences, row_width)
        parts = lax.all_to_all(stats, tensor_axes, split_axis=0, concat_axis=0, tiled=True)
        part_max, part_tot, part_wt, part_ch = parts[:, 0], parts[:, 1], parts[:, 2], parts[:, 3]
        overall = jnp.max(part_max, axis=0)
        factor = jnp.exp(part_max - overall[None])
        totals = jnp.sum(part_tot * factor, axis=0)
        weighted = jnp.sum(part_wt * factor, axis=0)
        chosen = jnp.sum(part_ch, axis=0)
        log_total = overall + jnp.log(totals)
        usable_rows = worker_marks >= 0
        log_prob = jnp.where(usable_rows, chosen - log_total, 0.0)
        entropy = jnp.where(usable_rows, log_total - weighted / totals, 0.0)

        both = jnp.stack([log_prob, entropy], axis=1)[arrived_slot]
        returned = lax.all_to_all(both, "dp", split_axis=0, concat_axis=0, tiled=True)[undo_order]
        return returned[:, 0], returned[:, 1]

    return local


def solution(mesh):
    split = split_tensor(mesh)
    if split is None:
        run_mesh, tensor_axes, tensor_size = mesh, ("tensor",), (mesh.shape["tensor"],)
    else:
        dp = mesh.shape["dp"]
        run_mesh = Mesh(mesh.devices.reshape(dp, split[0], split[1]), ("dp", "tx", "tz"))
        tensor_axes, tensor_size = ("tx", "tz"), split
    tensor = tensor_axes if len(tensor_axes) > 1 else tensor_axes[0]
    placed = (
        P("dp", tensor, None),
        P(),
        P(tensor, None),
        P("dp", tensor),
        P(),
        P("dp", tensor),
        P(),
    )
    return jax.shard_map(
        local_fn(tensor_axes, tensor_size),
        mesh=run_mesh,
        in_specs=placed,
        out_specs=(P("dp", tensor), P("dp", tensor)),
        check_vma=False,
    )
```

```python
import numpy as np
import jax
import jax.numpy as jnp
from jax import lax
from jax.experimental import pallas as pl
from jax.experimental.pallas import tpu as pltpu
from jax.sharding import Mesh
from jax.sharding import PartitionSpec as P

VREAL = 49155
INTERPRET = False
ROW_BLOCK = 256


def stats_kernel(offset_ref, emb_ref, rows_ref, marks_ref, out_ref):
    logits = lax.dot_general(
        emb_ref[...], rows_ref[...], (((1,), (1,)), ((), ())), preferred_element_type=jnp.float32
    )
    columns = offset_ref[0] + lax.broadcasted_iota(jnp.int32, (logits.shape[0], 1), 0)
    bias = jnp.where(columns < VREAL, 0.0, -jnp.inf)
    masked = logits + bias
    maximum = jnp.max(masked, axis=0, keepdims=True)
    shift = jnp.maximum(maximum, jnp.finfo(jnp.float32).min)
    weights = jnp.exp(masked - shift)
    totals = jnp.sum(weights, axis=0, keepdims=True)
    weighted = jnp.sum(weights * logits, axis=0, keepdims=True)
    chosen = jnp.sum(jnp.where(columns == marks_ref[...], logits, 0.0), axis=0, keepdims=True)
    out_ref[...] = jnp.concatenate([maximum, totals, weighted, chosen], axis=0)


def row_stats(rows, embedding, marks, offset):
    n, d = rows.shape
    v = embedding.shape[0]
    block = ROW_BLOCK if n % ROW_BLOCK == 0 else n
    return pl.pallas_call(
        stats_kernel,
        grid=(n // block,),
        in_specs=[
            pl.BlockSpec(memory_space=pltpu.SMEM),
            pl.BlockSpec((v, d), lambda i: (0, 0)),
            pl.BlockSpec((block, d), lambda i: (i, 0)),
            pl.BlockSpec((1, block), lambda i: (0, i)),
        ],
        out_specs=pl.BlockSpec((4, block), lambda i: (0, i)),
        out_shape=jax.ShapeDtypeStruct((4, n), jnp.float32),
        cost_estimate=pl.CostEstimate(
            flops=2 * n * v * d, transcendentals=n * v, bytes_accessed=2 * (n + v) * d + 20 * n
        ),
        interpret=INTERPRET,
    )(offset.reshape(1), embedding, rows, marks.reshape(1, n))


def normalize(hidden, norm_gain):
    values = hidden.astype(jnp.float32)
    inverse = lax.rsqrt(jnp.mean(values * values, axis=2, keepdims=True) + 1e-05)
    return (values * inverse * norm_gain).astype(jnp.bfloat16)


def split_tensor(mesh):
    row = mesh.devices[0]
    slow = len({tuple(d.coords)[0] for d in row})
    if row.size % slow or slow in (1, row.size):
        return None
    return slow, row.size // slow


def local_fn(tensor_axes, tensor_size):
    def tensor_rank():
        if len(tensor_axes) == 1:
            return lax.axis_index(tensor_axes[0])
        return lax.axis_index(tensor_axes[0]) * tensor_size[1] + lax.axis_index(tensor_axes[1])

    def gather_rows(normed):
        rows = normed
        for i, name in enumerate(tensor_axes):
            if i == 0 and len(tensor_axes) > 1:
                spread = jnp.broadcast_to(rows[None], (tensor_size[0],) + rows.shape)
                got = lax.all_to_all(spread, name, split_axis=0, concat_axis=0, tiled=True)
                rows = jnp.transpose(got, (1, 0, 2, 3)).reshape(rows.shape[0], -1, rows.shape[2])
            else:
                rows = lax.all_gather(rows, name, axis=1, tiled=True)
        return rows

    def to_gather_order(by_rank):
        s, w = by_rank.shape[1], by_rank.shape[2]
        if len(tensor_axes) == 1:
            return jnp.transpose(by_rank, (0, 2, 1)).reshape(-1)
        grid = by_rank.reshape(tensor_size[0], tensor_size[1], s, w)
        return jnp.transpose(grid, (1, 0, 3, 2)).reshape(-1)

    def from_gather_order(stats, s, w):
        k = stats.shape[0]
        if len(tensor_axes) == 1:
            return jnp.transpose(stats.reshape(k, tensor_size[0], w, s), (1, 0, 3, 2))
        grid = stats.reshape(k, tensor_size[1], tensor_size[0], w, s)
        grid = jnp.transpose(grid, (2, 1, 0, 4, 3))
        return grid.reshape(tensor_size[0] * tensor_size[1], k, s, w)

    def local(hidden, norm_gain, embedding, targets, lengths, loss_mask, deal_slots):
        group_rank = lax.axis_index("dp")
        sequences, row_width = hidden.shape[0], hidden.shape[1]
        ranks = int(np.prod(tensor_size))
        t_rank = tensor_rank()
        owned_seqs = group_rank * sequences + jnp.arange(sequences, dtype=jnp.int32)
        destination = deal_slots[owned_seqs] // sequences
        send_order = jnp.argsort(destination, stable=True)
        every_group = deal_slots // sequences
        arrived = jnp.argsort((every_group != group_rank).astype(jnp.int32), stable=True)[:sequences]
        arrived_slot = deal_slots[arrived] % sequences
        positions = t_rank * row_width + jnp.arange(row_width, dtype=jnp.int32)
        scored = (positions[None, :] < lengths[owned_seqs][:, None]) & (loss_mask == 1)
        marked = jnp.where(scored, targets, -1)
        undo_order = jnp.argsort(send_order)

        normed = normalize(hidden, norm_gain)
        row_block = gather_rows(normed)

        came = lax.all_to_all(marked[send_order], "dp", split_axis=0, concat_axis=0, tiled=True)
        worker_marks = came[jnp.argsort(arrived_slot)]
        spread = jnp.broadcast_to(worker_marks[None], (ranks,) + worker_marks.shape)
        block_marks = lax.all_to_all(spread, tensor_axes, split_axis=0, concat_axis=0, tiled=True)
        block_marks = to_gather_order(block_marks)

        offset = (t_rank * embedding.shape[0]).astype(jnp.int32)
        flat_rows = jnp.transpose(row_block, (1, 0, 2)).reshape(-1, row_block.shape[2])
        local_stats = row_stats(flat_rows, embedding, block_marks, offset)

        stats = from_gather_order(local_stats, sequences, row_width)
        parts = lax.all_to_all(stats, tensor_axes, split_axis=0, concat_axis=0, tiled=True)
        part_max, part_tot, part_wt, part_ch = parts[:, 0], parts[:, 1], parts[:, 2], parts[:, 3]
        overall = jnp.max(part_max, axis=0)
        factor = jnp.exp(part_max - overall[None])
        totals = jnp.sum(part_tot * factor, axis=0)
        weighted = jnp.sum(part_wt * factor, axis=0)
        chosen = jnp.sum(part_ch, axis=0)
        log_total = overall + jnp.log(totals)
        usable_rows = worker_marks >= 0
        log_prob = jnp.where(usable_rows, chosen - log_total, 0.0)
        entropy = jnp.where(usable_rows, log_total - weighted / totals, 0.0)

        both = jnp.stack([log_prob, entropy], axis=1)[arrived_slot]
        returned = lax.all_to_all(both, "dp", split_axis=0, concat_axis=0, tiled=True)[undo_order]
        return returned[:, 0], returned[:, 1]

    return local


def solution(mesh):
    split = split_tensor(mesh)
    if split is None:
        run_mesh, tensor_axes, tensor_size = mesh, ("tensor",), (mesh.shape["tensor"],)
    else:
        dp = mesh.shape["dp"]
        run_mesh = Mesh(mesh.devices.reshape(dp, split[0], split[1]), ("dp", "tx", "tz"))
        tensor_axes, tensor_size = ("tx", "tz"), split
    tensor = tensor_axes if len(tensor_axes) > 1 else tensor_axes[0]
    placed = (
        P("dp", tensor, None),
        P(),
        P(tensor, None),
        P("dp", tensor),
        P(),
        P("dp", tensor),
        P(),
    )
    return jax.shard_map(
        local_fn(tensor_axes, tensor_size),
        mesh=run_mesh,
        in_specs=placed,
        out_specs=(P("dp", tensor), P("dp", tensor)),
        check_vma=False,
    )
```
